32 devices in a mesh: dp: 8 (over z, y), ctx: 4 (over x, core).
Axes of the slice: x: 2, y: 2, z: 4, core: 2. Of those that a mesh axis runs over, the one named last changes fastest.
Arguments:
- queries: bfloat16 [4096, 4096], P(('dp', 'ctx')), may hold values from -40 to 40
- key_head_inputs: bfloat16 [4096, 512], P(('dp', 'ctx')), may hold values from -40 to 40
- value_head_inputs: bfloat16 [4096, 512], P(('dp', 'ctx')), may hold values from -6 to 6
- output_gradient: bfloat16 [4096, 4096], P(('dp', 'ctx')), may hold values from -6 to 6
- positions: int32 [4096], P(('dp', 'ctx')), may hold values from 0 to 1023, as said below
- counts: int32 [32], P(('dp', 'ctx')), may hold values from 64 to 128, as said below
- inputs: bfloat16 [4096, 8192], P(('dp', 'ctx')), may hold values from -6 to 6
Outputs:
- query_grad: bfloat16 [4096, 4096], P(('dp', 'ctx'))
- key_grad: bfloat16 [4096, 512], P(('dp', 'ctx'))
- value_grad: bfloat16 [4096, 512], P(('dp', 'ctx'))
- value_weight_gradient: float32 [512, 8192], P('dp', 'ctx')
The draws below stay inside these ranges and needn't reach their ends.
Inputs may be any that keep to these rules, and one draw needn't show every extreme that they name: A device's valid slots are its first counts slots; the others are padding. Some device holds 128 valid slots. Along a sequence the positions of valid slots rise strictly; the first slot holds 0 and the last valid slot 1023. A padding slot repeats the position before it, or holds 1023 after the last valid slot.
All inputs are finite; a program needn't handle non-finite values.
Results may differ from the reference program's by a relative error of at most 0.0061.
Values may be sent and summed in bfloat16 or wider, within the bound.
No kernel may reach another device: no remote copies, remote signals or barrier semaphores. Data moves between devices by JAX's collectives and lax.ppermute only.
A program may use at most 128 MiB of HBM per device.

```python
import math
import jax
import jax.numpy as jnp
from jax import lax

MODEL_DIM = 8192
HEAD_DIM = 128
QUERY_HEADS = 32
KEY_HEADS = 4
DEVICE_ROWS = 128
KVW = 512
KEPT_PER_SEQ = 512
CONTEXT = 1024
KEPT_TOTAL = 4096
N_CTX = 4


def count_table(key):
    device_total = KEPT_TOTAL // DEVICE_ROWS
    drawn = jax.random.randint(jax.random.fold_in(key, 11), (device_total,), DEVICE_ROWS // 2, DEVICE_ROWS + 1)
    full_device = jax.random.randint(jax.random.fold_in(key, 12), (), 0, device_total)
    return jnp.where(jnp.arange(device_total) == full_device, DEVICE_ROWS, drawn).astype(jnp.int32)


def draw_counts(key, part):
    return count_table(key)


def draw_positions(key, part):
    count_row = count_table(key)
    sequence_total = KEPT_TOTAL // KEPT_PER_SEQ
    slot_index = jnp.arange(KEPT_TOTAL, dtype=jnp.int32) % DEVICE_ROWS
    is_valid = slot_index < jnp.repeat(count_row, DEVICE_ROWS)
    gap_sizes = jax.random.randint(jax.random.fold_in(key, 13), (KEPT_TOTAL,), 1, 3)
    gap_sizes = jnp.where(is_valid, gap_sizes, 0).reshape(sequence_total, KEPT_PER_SEQ)
    seq_slots = jnp.arange(KEPT_PER_SEQ, dtype=jnp.int32)
    gap_sizes = jnp.where(seq_slots[None, :] == 0, 1, gap_sizes)
    position = jnp.cumsum(gap_sizes, axis=1) - 1
    last_count = count_row.reshape(sequence_total, KEPT_PER_SEQ // DEVICE_ROWS)[:, -1]
    last_slot = KEPT_PER_SEQ - DEVICE_ROWS + last_count - 1
    position = jnp.where(seq_slots[None, :] >= last_slot[:, None], CONTEXT - 1, position)
    return position.reshape(KEPT_TOTAL).astype(jnp.int32)


def query_key_pair(key):
    query_sample = jnp.clip(jax.random.normal(jax.random.fold_in(key, 21), (KEPT_TOTAL, QUERY_HEADS, HEAD_DIM), jnp.float32), -4.0, 4.0)
    key_sample = jnp.clip(jax.random.normal(jax.random.fold_in(key, 22), (KEPT_TOTAL, KEY_HEADS, HEAD_DIM), jnp.float32), -4.0, 4.0)
    return (query_sample.reshape(KEPT_TOTAL, QUERY_HEADS * HEAD_DIM), key_sample.reshape(KEPT_TOTAL, KEY_HEADS * HEAD_DIM))


def draw_queries(key, part):
    return query_key_pair(key)[0].astype(jnp.bfloat16)


def draw_key_head_inputs(key, part):
    return query_key_pair(key)[1].astype(jnp.bfloat16)


def spiked(array, key, source, target, blocks, factor):
    owner, partner = [(jnp.arange(array.shape[dim]) // (array.shape[dim] // blocks)).reshape([-1 if axis == dim else 1 for axis in range(array.ndim)]) for dim in (source, target)]
    chosen = jax.random.permutation(key, blocks)[partner]
    strong = (owner == chosen) | (owner == (partner + blocks // 2) % blocks)
    return jnp.where(strong, factor * array, array)


def block_levels(key, shape, split, smallest, largest):
    def one(axis_at, shards_of):
        heights = jax.random.uniform(jax.random.fold_in(jax.random.fold_in(key, 6), axis_at), (shards_of,), jnp.float32, smallest / len(split), largest / len(split))
        return jnp.repeat(jnp.exp(heights), shape[axis_at] // shards_of).reshape((-1,) + (1,) * (len(shape) - axis_at - 1))

    level = one(*split[0])
    for cut in split[1:]:
        level = level * one(*cut)
    return level


def normal_values(rng, shape, scale, reach, cuts=(), held_as=jnp.bfloat16):
    values = jax.random.normal(rng, shape, jnp.float32) * scale
    if len(cuts) > 0:
        values = block_levels(rng, shape, cuts, -0.22, 0.18) * values
    return jnp.clip(values, min=-reach, max=reach).astype(held_as)


def gaussian_with(rng, shape, spread, reach, split, heavy, kind=jnp.bfloat16):
    entries = spread * jax.random.normal(rng, shape, jnp.float32)
    if split:
        entries = entries * block_levels(rng, shape, split, -0.22, 0.18)
    return jnp.clip(spiked(entries, jax.random.fold_in(rng, 3), *heavy), -reach, reach).astype(kind)


def setup_inputs(seed: int = 0) -> dict:
    key_list = jax.random.split(jax.random.key(seed), 8)
    return {
        "queries": draw_queries(jax.random.fold_in(key_list[7], 71), 0),
        "key_head_inputs": draw_key_head_inputs(jax.random.fold_in(key_list[7], 71), 0),
        "value_head_inputs": normal_values(key_list[2], (KEPT_TOTAL, KVW), 1.0, 6.0, ((0, 32),)),
        "output_gradient": normal_values(key_list[3], (KEPT_TOTAL, QUERY_HEADS * HEAD_DIM), 1.0, 6.0, ((0, 32),)),
        "positions": draw_positions(jax.random.fold_in(key_list[7], 71), 0),
        "counts": draw_counts(jax.random.fold_in(key_list[7], 71), 0),
        "inputs": gaussian_with(key_list[6], (KEPT_TOTAL, MODEL_DIM), 1.0, 6.0, ((0, 32),), (0, 1, 32, 2.75)),
    }


THETA = 500000.0

def rope_tables(position, head_size):
    half_width = head_size // 2
    frequency = jnp.exp(jnp.arange(half_width, dtype=jnp.float32) * (-2.0 * math.log(THETA) / head_size))
    angles = position.astype(jnp.float32)[:, None] * frequency[None, :]
    return (jnp.cos(angles), jnp.sin(angles))

def apply_rotation(vectors, cosine_table, sine_lookup, sense):
    half_width = vectors.shape[-1] // 2
    lower_half = vectors[..., :half_width]
    upper_half = vectors[..., half_width:]
    cos_part = cosine_table[:, None, :]
    sin_part = sine_lookup[:, None, :] * sense
    return jnp.concatenate([lower_half * cos_part - upper_half * sin_part, upper_half * cos_part + lower_half * sin_part], axis=-1)

def to_bf16_float(values_in):
    return lax.optimization_barrier(values_in.astype(jnp.bfloat16)).astype(jnp.float32)

def reference(queries, key_head_inputs, value_head_inputs, output_gradient, positions, counts, inputs):
    query_group_width = QUERY_HEADS // KEY_HEADS
    score_scale = 1.0 / math.sqrt(HEAD_DIM)
    sequence_total = KEPT_TOTAL // KEPT_PER_SEQ

    def sequence_count(weight_sum, element_count):
        q_seq, key_sequence, value_sequence, output_grad_sequence, pos_seq, count_row, x_seq = element_count
        cosine_table, sine_lookup = rope_tables(pos_seq, HEAD_DIM)
        query_rotated = apply_rotation(q_seq.reshape(KEPT_PER_SEQ, QUERY_HEADS, HEAD_DIM).astype(jnp.float32), cosine_table, sine_lookup, 1.0).astype(jnp.bfloat16)
        key_rotated = apply_rotation(key_sequence.reshape(KEPT_PER_SEQ, KEY_HEADS, HEAD_DIM).astype(jnp.float32), cosine_table, sine_lookup, 1.0).astype(jnp.bfloat16)
        slot_ids = jnp.arange(KEPT_PER_SEQ, dtype=jnp.int32)
        is_valid = slot_ids % DEVICE_ROWS < jnp.repeat(count_row, DEVICE_ROWS)
        key_float = key_rotated.astype(jnp.float32)
        value_single_precision = value_sequence.reshape(KEPT_PER_SEQ, KEY_HEADS, HEAD_DIM).astype(jnp.float32)
        query_blocks = query_rotated.reshape(N_CTX, DEVICE_ROWS, KEY_HEADS, query_group_width, HEAD_DIM)
        output_grad_blocks = output_grad_sequence.reshape(N_CTX, DEVICE_ROWS, KEY_HEADS, query_group_width, HEAD_DIM)
        pos_blocks = pos_seq.reshape(N_CTX, DEVICE_ROWS)
        valid_blocks = is_valid.reshape(N_CTX, DEVICE_ROWS)

        def per_block(carry, block_items):
            key_accumulator, value_accumulator = carry
            q_block, do_block, q_pos, q_valid = block_items
            q_float = q_block.astype(jnp.float32)
            do_float = do_block.astype(jnp.float32)
            scores = jnp.einsum('qhgd,khd->hgqk', q_float, key_float) * score_scale
            allowed = q_valid[:, None] & is_valid[None, :] & (pos_seq[None, :] <= q_pos[:, None])
            row_top = lax.optimization_barrier(jnp.max(jnp.where(allowed, scores, -1e+30), axis=-1))
            exp_terms = jnp.where(allowed, jnp.exp(scores - row_top[..., None]), 0.0)
            denominator = jnp.where(q_valid[None, None, :], lax.optimization_barrier(jnp.sum(exp_terms, axis=-1)), 1.0)
            softmax = exp_terms / denominator[..., None]
            d_probs = jnp.einsum('qhgd,khd->hgqk', do_float, value_single_precision)
            row_delta = lax.optimization_barrier(jnp.sum(softmax * d_probs, axis=-1))
            d_scores = softmax * (d_probs - row_delta[..., None]) * score_scale
            prob_bf = to_bf16_float(softmax)
            dscore_bf = to_bf16_float(d_scores)
            q_grad = jnp.einsum('hgqk,khd->qhgd', dscore_bf, key_float)
            key_accumulator = key_accumulator + jnp.einsum('hgqk,qhgd->khd', dscore_bf, q_float)
            value_accumulator = value_accumulator + jnp.einsum('hgqk,qhgd->khd', prob_bf, do_float)
            return ((key_accumulator, value_accumulator), q_grad)
        initial_gradients = jnp.zeros((KEPT_PER_SEQ, KEY_HEADS, HEAD_DIM), jnp.float32)
        (key_accumulator, value_accumulator), q_grads = lax.scan(per_block, (initial_gradients, initial_gradients), (query_blocks, output_grad_blocks, pos_blocks, valid_blocks))
        q_grad = apply_rotation(q_grads.reshape(KEPT_PER_SEQ, QUERY_HEADS, HEAD_DIM), cosine_table, sine_lookup, -1.0).astype(jnp.bfloat16).reshape(KEPT_PER_SEQ, QUERY_HEADS * HEAD_DIM)
        key_gradient = apply_rotation(key_accumulator, cosine_table, sine_lookup, -1.0).astype(jnp.bfloat16).reshape(KEPT_PER_SEQ, KEY_HEADS * HEAD_DIM)
        value_gradient = value_accumulator.astype(jnp.bfloat16).reshape(KEPT_PER_SEQ, KEY_HEADS * HEAD_DIM)
        weight_sum = weight_sum + jnp.dot(value_gradient.T, x_seq, preferred_element_type=jnp.float32)
        return (weight_sum, (q_grad, key_gradient, value_gradient))
    element_count = (queries.reshape(sequence_total, KEPT_PER_SEQ, QUERY_HEADS * HEAD_DIM), key_head_inputs.reshape(sequence_total, KEPT_PER_SEQ, KEY_HEADS * HEAD_DIM), value_head_inputs.reshape(sequence_total, KEPT_PER_SEQ, KEY_HEADS * HEAD_DIM), output_gradient.reshape(sequence_total, KEPT_PER_SEQ, QUERY_HEADS * HEAD_DIM), positions.reshape(sequence_total, KEPT_PER_SEQ), counts.reshape(sequence_total, N_CTX), inputs.reshape(sequence_total, KEPT_PER_SEQ, MODEL_DIM))
    value_weight_gradient, (query_everything, key_everything, value_everything) = lax.scan(sequence_count, jnp.zeros((KEY_HEADS * HEAD_DIM, MODEL_DIM), jnp.float32), element_count)
    return (query_everything.reshape(KEPT_TOTAL, QUERY_HEADS * HEAD_DIM), key_everything.reshape(KEPT_TOTAL, KEY_HEADS * HEAD_DIM), value_everything.reshape(KEPT_TOTAL, KEY_HEADS * HEAD_DIM), value_weight_gradient)
```

```python
import math

import jax
import jax.numpy as jnp
from jax import lax
from jax.sharding import PartitionSpec as P

HEAD_DIM = 128
QUERY_HEADS = 32
KEY_HEADS = 4


THETA = 500000.0


def rope_tables(position, head_size):
    half_width = head_size // 2
    frequency = jnp.exp(
        jnp.arange(half_width, dtype=jnp.float32) * (-2.0 * math.log(THETA) / head_size)
    )
    angles = position.astype(jnp.float32)[:, None] * frequency[None, :]
    return (jnp.cos(angles), jnp.sin(angles))


def apply_rotation(vectors, cosine_table, sine_lookup, sense):
    half_width = vectors.shape[-1] // 2
    lower_half = vectors[..., :half_width]
    upper_half = vectors[..., half_width:]
    cos_part = cosine_table[:, None, :]
    sin_part = sine_lookup[:, None, :] * sense
    return jnp.concatenate(
        [
            lower_half * cos_part - upper_half * sin_part,
            upper_half * cos_part + lower_half * sin_part,
        ],
        axis=-1,
    )


def per_device(
    queries, key_head_inputs, value_head_inputs, output_gradient, positions, counts, inputs
):
    row_number_total = queries.shape[0]
    query_group_width = QUERY_HEADS // KEY_HEADS
    axis_span = lax.axis_size("ctx")
    retained_slots = row_number_total * axis_span
    key_block = min(512, retained_slots)
    my_index = lax.axis_index("ctx")
    score_scale = 1.0 / math.sqrt(HEAD_DIM)
    cosine_table, sine_lookup = rope_tables(positions, HEAD_DIM)
    column_inputs = lax.all_to_all(inputs, "ctx", 1, 0, tiled=True)
    query_rotated = apply_rotation(
        queries.reshape(row_number_total, QUERY_HEADS, HEAD_DIM).astype(jnp.float32),
        cosine_table,
        sine_lookup,
        1.0,
    ).astype(jnp.bfloat16)
    key_rotated = apply_rotation(
        key_head_inputs.reshape(row_number_total, KEY_HEADS, HEAD_DIM).astype(jnp.float32),
        cosine_table,
        sine_lookup,
        1.0,
    ).astype(jnp.bfloat16)
    key_rotated = key_rotated.reshape(row_number_total, KEY_HEADS * HEAD_DIM)
    key_row_block, value_row_block, all_counts = (
        lax.all_gather(key_rotated, "ctx", axis=0, tiled=True),
        lax.all_gather(value_head_inputs, "ctx", axis=0, tiled=True),
        lax.all_gather(counts, "ctx", axis=0, tiled=True),
    )
    gathered_keys = key_row_block.reshape(retained_slots, KEY_HEADS, HEAD_DIM)
    gathered_values = value_row_block.reshape(retained_slots, KEY_HEADS, HEAD_DIM)
    key_valid = jnp.arange(retained_slots, dtype=jnp.int32) % row_number_total < jnp.repeat(
        all_counts, row_number_total
    )
    own_valid = jnp.arange(row_number_total, dtype=jnp.int32) < counts[0]
    initial_gradients = jnp.zeros((retained_slots, KEY_HEADS, HEAD_DIM), jnp.float32)
    first_slot = my_index * row_number_total
    key_accumulator = initial_gradients
    value_accumulator = initial_gradients
    query_count = query_rotated.shape[0]
    query_grouped = query_rotated.reshape(query_count, KEY_HEADS, query_group_width, HEAD_DIM)
    output_grad_grouped = output_gradient.reshape(
        query_count, KEY_HEADS, query_group_width, HEAD_DIM
    )
    q_slots = first_slot + jnp.arange(query_count, dtype=jnp.int32)
    block_total = (first_slot + query_count - 1) // key_block + 1

    def scores_for(begin_at):
        k_blk = lax.dynamic_slice_in_dim(gathered_keys, begin_at, key_block, 0)
        v_blk = lax.dynamic_slice_in_dim(gathered_values, begin_at, key_block, 0)
        k_slots = begin_at + jnp.arange(key_block, dtype=jnp.int32)
        k_valid = lax.dynamic_slice_in_dim(key_valid, begin_at, key_block, 0)
        allowed = own_valid[:, None] & k_valid[None, :] & (k_slots[None, :] <= q_slots[:, None])
        scores = (
            jnp.einsum("qhgd,khd->hgqk", query_grouped, k_blk, preferred_element_type=jnp.float32)
            * score_scale
        )
        d_probs = jnp.einsum(
            "qhgd,khd->hgqk", output_grad_grouped, v_blk, preferred_element_type=jnp.float32
        )
        return (k_blk, scores, d_probs, allowed)

    def first_pass(step_index, carry):
        row_top, row_total, weighted = carry
        k_blk, scores, d_probs, allowed = scores_for(step_index * key_block)
        new_top = jnp.maximum(row_top, jnp.max(jnp.where(allowed, scores, -1e30), axis=-1))
        factor = jnp.exp(row_top - new_top)
        exp_terms = jnp.where(allowed, jnp.exp(scores - new_top[..., None]), 0.0)
        return (
            new_top,
            row_total * factor + jnp.sum(exp_terms, axis=-1),
            weighted * factor + jnp.sum(exp_terms * d_probs, axis=-1),
        )

    statistic_shape = (KEY_HEADS, query_group_width, query_count)
    start_stats = (
        jnp.full(statistic_shape, -1e30, jnp.float32),
        jnp.zeros(statistic_shape, jnp.float32),
        jnp.zeros(statistic_shape, jnp.float32),
    )
    row_top, row_total, weighted = lax.fori_loop(0, block_total, first_pass, start_stats)
    row_total = jnp.where(own_valid[None, None, :], row_total, 1.0)
    row_delta = weighted / row_total

    def second_pass(step_index, carry):
        q_acc, key_sum, value_sum = carry
        begin_at = step_index * key_block
        k_blk, scores, d_probs, allowed = scores_for(begin_at)
        softmax = (
            jnp.where(allowed, jnp.exp(scores - row_top[..., None]), 0.0) / row_total[..., None]
        )
        d_scores = softmax * (d_probs - row_delta[..., None]) * score_scale
        prob_bf = softmax.astype(jnp.bfloat16)
        dscore_bf = d_scores.astype(jnp.bfloat16)
        q_acc = q_acc + jnp.einsum(
            "hgqk,khd->qhgd", dscore_bf, k_blk, preferred_element_type=jnp.float32
        )
        k_piece = jnp.einsum(
            "hgqk,qhgd->khd", dscore_bf, query_grouped, preferred_element_type=jnp.float32
        )
        v_piece = jnp.einsum(
            "hgqk,qhgd->khd", prob_bf, output_grad_grouped, preferred_element_type=jnp.float32
        )
        key_sum = lax.dynamic_update_slice_in_dim(
            key_sum,
            lax.dynamic_slice_in_dim(key_sum, begin_at, key_block, 0) + k_piece,
            begin_at,
            0,
        )
        value_sum = lax.dynamic_update_slice_in_dim(
            value_sum,
            lax.dynamic_slice_in_dim(value_sum, begin_at, key_block, 0) + v_piece,
            begin_at,
            0,
        )
        return (q_acc, key_sum, value_sum)

    query_offset = jnp.zeros((query_count, KEY_HEADS, query_group_width, HEAD_DIM), jnp.float32)
    q_acc, key_accumulator, value_accumulator = lax.fori_loop(
        0, block_total, second_pass, (query_offset, key_accumulator, value_accumulator)
    )
    q_grad_rot, key_accumulator, value_accumulator = (
        q_acc.reshape(query_count, QUERY_HEADS, HEAD_DIM),
        key_accumulator,
        value_accumulator,
    )
    key_portion, value_part = (
        lax.psum_scatter(
            key_accumulator.reshape(retained_slots, KEY_HEADS * HEAD_DIM),
            "ctx",
            scatter_dimension=0,
            tiled=True,
        ),
        lax.psum_scatter(
            value_accumulator.reshape(retained_slots, KEY_HEADS * HEAD_DIM),
            "ctx",
            scatter_dimension=0,
            tiled=True,
        ),
    )
    query_grad = (
        apply_rotation(q_grad_rot, cosine_table, sine_lookup, -1.0)
        .astype(jnp.bfloat16)
        .reshape(row_number_total, QUERY_HEADS * HEAD_DIM)
    )
    key_grad = (
        apply_rotation(
            key_portion.reshape(row_number_total, KEY_HEADS, HEAD_DIM),
            cosine_table,
            sine_lookup,
            -1.0,
        )
        .astype(jnp.bfloat16)
        .reshape(row_number_total, KEY_HEADS * HEAD_DIM)
    )
    value_grad = value_part.astype(jnp.bfloat16)
    sequence_grad = lax.all_gather(value_grad, "ctx", axis=0, tiled=True)
    weight_part = lax.dot_general(
        sequence_grad, column_inputs, (((0,), (0,)), ((), ())), preferred_element_type=jnp.float32
    )
    shares = lax.psum_scatter(weight_part, "dp", scatter_dimension=0, tiled=True)
    return (query_grad, key_grad, value_grad, shares)


def solution(mesh):
    placed = (
        P(("dp", "ctx"), None),
        P(("dp", "ctx"), None),
        P(("dp", "ctx"), None),
        P(("dp", "ctx"), None),
        P(("dp", "ctx")),
        P(("dp", "ctx")),
        P(("dp", "ctx"), None),
    )
    return jax.shard_map(
        per_device,
        mesh=mesh,
        in_specs=placed,
        out_specs=(
            P(("dp", "ctx"), None),
            P(("dp", "ctx"), None),
            P(("dp", "ctx"), None),
            P("dp", "ctx"),
        ),
        check_vma=False,
    )
```

```python
import math

import jax
import jax.numpy as jnp
from jax import lax
from jax.sharding import PartitionSpec as P

HEAD_DIM = 128
QUERY_HEADS = 32
KEY_HEADS = 4


THETA = 500000.0


def rope_tables(position, head_size):
    half_width = head_size // 2
    frequency = jnp.exp(
        jnp.arange(half_width, dtype=jnp.float32) * (-2.0 * math.log(THETA) / head_size)
    )
    angles = position.astype(jnp.float32)[:, None] * frequency[None, :]
    return (jnp.cos(angles), jnp.sin(angles))


def apply_rotation(vectors, cosine_table, sine_lookup, sense):
    half_width = vectors.shape[-1] // 2
    lower_half = vectors[..., :half_width]
    upper_half = vectors[..., half_width:]
    cos_part = cosine_table[:, None, :]
    sin_part = sine_lookup[:, None, :] * sense
    return jnp.concatenate(
        [
            lower_half * cos_part - upper_half * sin_part,
            upper_half * cos_part + lower_half * sin_part,
        ],
        axis=-1,
    )


def per_device(
    queries, key_head_inputs, value_head_inputs, output_gradient, positions, counts, inputs
):
    row_number_total = queries.shape[0]
    query_group_width = QUERY_HEADS // KEY_HEADS
    axis_span = lax.axis_size("ctx")
    retained_slots = row_number_total * axis_span
    key_block = min(512, retained_slots)
    my_index = lax.axis_index("ctx")
    score_scale = 1.0 / math.sqrt(HEAD_DIM)
    cosine_table, sine_lookup = rope_tables(positions, HEAD_DIM)
    column_inputs = lax.all_to_all(inputs, "ctx", 1, 0, tiled=True)
    query_rotated = apply_rotation(
        queries.reshape(row_number_total, QUERY_HEADS, HEAD_DIM).astype(jnp.float32),
        cosine_table,
        sine_lookup,
        1.0,
    ).astype(jnp.bfloat16)
    key_rotated = apply_rotation(
        key_head_inputs.reshape(row_number_total, KEY_HEADS, HEAD_DIM).astype(jnp.float32),
        cosine_table,
        sine_lookup,
        1.0,
    ).astype(jnp.bfloat16)
    key_rotated = key_rotated.reshape(row_number_total, KEY_HEADS * HEAD_DIM)
    key_row_block, value_row_block, all_counts = (
        lax.all_gather(key_rotated, "ctx", axis=0, tiled=True),
        lax.all_gather(value_head_inputs, "ctx", axis=0, tiled=True),
        lax.all_gather(counts, "ctx", axis=0, tiled=True),
    )
    gathered_keys = key_row_block.reshape(retained_slots, KEY_HEADS, HEAD_DIM)
    gathered_values = value_row_block.reshape(retained_slots, KEY_HEADS, HEAD_DIM)
    key_valid = jnp.arange(retained_slots, dtype=jnp.int32) % row_number_total < jnp.repeat(
        all_counts, row_number_total
    )
    own_valid = jnp.arange(row_number_total, dtype=jnp.int32) < counts[0]
    initial_gradients = jnp.zeros((retained_slots, KEY_HEADS, HEAD_DIM), jnp.float32)
    first_slot = my_index * row_number_total
    key_accumulator = initial_gradients
    value_accumulator = initial_gradients
    query_count = query_rotated.shape[0]
    query_grouped = query_rotated.reshape(query_count, KEY_HEADS, query_group_width, HEAD_DIM)
    output_grad_grouped = output_gradient.reshape(
        query_count, KEY_HEADS, query_group_width, HEAD_DIM
    )
    q_slots = first_slot + jnp.arange(query_count, dtype=jnp.int32)
    block_total = (first_slot + query_count - 1) // key_block + 1

    def scores_for(begin_at):
        k_blk = lax.dynamic_slice_in_dim(gathered_keys, begin_at, key_block, 0)
        v_blk = lax.dynamic_slice_in_dim(gathered_values, begin_at, key_block, 0)
        k_slots = begin_at + jnp.arange(key_block, dtype=jnp.int32)
        k_valid = lax.dynamic_slice_in_dim(key_valid, begin_at, key_block, 0)
        allowed = own_valid[:, None] & k_valid[None, :] & (k_slots[None, :] <= q_slots[:, None])
        scores = (
            jnp.einsum("qhgd,khd->hgqk", query_grouped, k_blk, preferred_element_type=jnp.float32)
            * score_scale
        )
        d_probs = jnp.einsum(
            "qhgd,khd->hgqk", output_grad_grouped, v_blk, preferred_element_type=jnp.float32
        )
        return (k_blk, scores, d_probs, allowed)

    def first_pass(step_index, carry):
        row_top, row_total, weighted = carry
        k_blk, scores, d_probs, allowed = scores_for(step_index * key_block)
        new_top = jnp.maximum(row_top, jnp.max(jnp.where(allowed, scores, -1e30), axis=-1))
        factor = jnp.exp(row_top - new_top)
        exp_terms = jnp.where(allowed, jnp.exp(scores - new_top[..., None]), 0.0)
        return (
            new_top,
            row_total * factor + jnp.sum(exp_terms, axis=-1),
            weighted * factor + jnp.sum(exp_terms * d_probs, axis=-1),
        )

    statistic_shape = (KEY_HEADS, query_group_width, query_count)
    start_stats = (
        jnp.full(statistic_shape, -1e30, jnp.float32),
        jnp.zeros(statistic_shape, jnp.float32),
        jnp.zeros(statistic_shape, jnp.float32),
    )
    row_top, row_total, weighted = lax.fori_loop(0, block_total, first_pass, start_stats)
    row_total = jnp.where(own_valid[None, None, :], row_total, 1.0)
    row_delta = weighted / row_total

    def second_pass(step_index, carry):
        q_acc, key_sum, value_sum = carry
        begin_at = step_index * key_block
        k_blk, scores, d_probs, allowed = scores_for(begin_at)
        softmax = (
            jnp.where(allowed, jnp.exp(scores - row_top[..., None]), 0.0) / row_total[..., None]
        )
        d_scores = softmax * (d_probs - row_delta[..., None]) * score_scale
        prob_bf = softmax.astype(jnp.bfloat16)
        dscore_bf = d_scores.astype(jnp.bfloat16)
        q_acc = q_acc + jnp.einsum(
            "hgqk,khd->qhgd", dscore_bf, k_blk, preferred_element_type=jnp.float32
        )
        k_piece = jnp.einsum(
            "hgqk,qhgd->khd", dscore_bf, query_grouped, preferred_element_type=jnp.float32
        )
        v_piece = jnp.einsum(
            "hgqk,qhgd->khd", prob_bf, output_grad_grouped, preferred_element_type=jnp.float32
        )
        key_sum = lax.dynamic_update_slice_in_dim(
            key_sum,
            lax.dynamic_slice_in_dim(key_sum, begin_at, key_block, 0) + k_piece,
            begin_at,
            0,
        )
        value_sum = lax.dynamic_update_slice_in_dim(
            value_sum,
            lax.dynamic_slice_in_dim(value_sum, begin_at, key_block, 0) + v_piece,
            begin_at,
            0,
        )
        return (q_acc, key_sum, value_sum)

    query_offset = jnp.zeros((query_count, KEY_HEADS, query_group_width, HEAD_DIM), jnp.float32)
    q_acc, key_accumulator, value_accumulator = lax.fori_loop(
        0, block_total, second_pass, (query_offset, key_accumulator, value_accumulator)
    )
    q_grad_rot, key_accumulator, value_accumulator = (
        q_acc.reshape(query_count, QUERY_HEADS, HEAD_DIM),
        key_accumulator,
        value_accumulator,
    )
    key_portion, value_part = (
        lax.psum_scatter(
            key_accumulator.reshape(retained_slots, KEY_HEADS * HEAD_DIM),
            "ctx",
            scatter_dimension=0,
            tiled=True,
        ),
        lax.psum_scatter(
            value_accumulator.reshape(retained_slots, KEY_HEADS * HEAD_DIM),
            "ctx",
            scatter_dimension=0,
            tiled=True,
        ),
    )
    query_grad = (
        apply_rotation(q_grad_rot, cosine_table, sine_lookup, -1.0)
        .astype(jnp.bfloat16)
        .reshape(row_number_total, QUERY_HEADS * HEAD_DIM)
    )
    key_grad = (
        apply_rotation(
            key_portion.reshape(row_number_total, KEY_HEADS, HEAD_DIM),
            cosine_table,
            sine_lookup,
            -1.0,
        )
        .astype(jnp.bfloat16)
        .reshape(row_number_total, KEY_HEADS * HEAD_DIM)
    )
    value_grad = value_part.astype(jnp.bfloat16)
    sequence_grad = lax.all_gather(value_grad, "ctx", axis=0, tiled=True)
    weight_part = lax.dot_general(
        sequence_grad, column_inputs, (((0,), (0,)), ((), ())), preferred_element_type=jnp.float32
    )
    dp_span = lax.axis_size("dp")
    pieces = lax.all_to_all(
        weight_part.reshape(dp_span, weight_part.shape[0] // dp_span, weight_part.shape[1]),
        "dp",
        0,
        0,
        tiled=True,
    )
    shares = jnp.sum(pieces, axis=0)
    return (query_grad, key_grad, value_grad, shares)


def solution(mesh):
    placed = (
        P(("dp", "ctx"), None),
        P(("dp", "ctx"), None),
        P(("dp", "ctx"), None),
        P(("dp", "ctx"), None),
        P(("dp", "ctx")),
        P(("dp", "ctx")),
        P(("dp", "ctx"), None),
    )
    return jax.shard_map(
        per_device,
        mesh=mesh,
        in_specs=placed,
        out_specs=(
            P(("dp", "ctx"), None),
            P(("dp", "ctx"), None),
            P(("dp", "ctx"), None),
            P("dp", "ctx"),
        ),
        check_vma=False,
    )
```
